512 devices in a mesh: mpo: 8 (over y, core), sec: 64 (over x, z).
Axes of the slice: x: 4, y: 4, z: 16, core: 2. Of those that a mesh axis runs over, the one named last changes fastest.
Arguments:
- theta: bfloat16 [16, 1024, 1024], P(None, 'sec'), may hold values from -6 to 6
- env_left: bfloat16 [24, 16384, 1024], P('mpo', 'sec'), may hold values from -0.1875 to 0.1875
- env_right: bfloat16 [24, 16384, 1024], P('mpo', 'sec'), may hold values from -0.0390625 to 0.0390625
- mpo_core: float32 [24, 24], replicated, may hold values from -1.25 to 1.25
- sector_sizes: int32 [16], replicated, may hold values from 1 to 1024, 12288 in all
Outputs:
- applied: bfloat16 [1024, 16384], P('mpo', 'sec')
The draws below stay inside these ranges and needn't reach their ends.
Inputs may be any that keep to these rules, and one draw needn't show every extreme that they name: `sector_sizes`: one sector has exactly 1024 states in use; the sizes sum to 12288.
All inputs are finite; a program needn't handle non-finite values.
Results may differ from the reference program's by a relative error of at most 0.0058.
Values may be sent and summed in bfloat16 or wider, within the bound.
No kernel may reach another device: no remote copies, remote signals or barrier semaphores. Data moves between devices by JAX's collectives and lax.ppermute only.
A program may use at most 64 MiB of HBM per device.

```python
import math
import jax
import jax.numpy as jnp
import numpy as np
from jax import lax

M = 1024
W = 24
S = 16


def steps_of(rng, shape, cuts, smallest, top_value):
    gain, own = 1.0, jax.random.fold_in(rng, 6)
    for axis_at, blocks in cuts:
        steps = jnp.exp(jax.random.uniform(jax.random.fold_in(own, axis_at), (blocks,), jnp.float32, smallest / len(cuts), top_value / len(cuts)))
        gain = gain * jnp.repeat(steps, shape[axis_at] // blocks).reshape([-1 if axis == axis_at else 1 for axis in range(len(shape))])
    return gain


def split_up(number_of, total, limit, lean):
    weights = [(1 << 20) // math.isqrt(rank ** lean) + 1 for rank in range(2, number_of + 1)]
    surplus, holding = total - limit - (number_of - 1), [1] * (number_of - 1)
    while surplus > 0:
        candidates = [i for i in range(number_of - 1) if holding[i] < limit]
        pool, remaining = sum([weights[i] for i in candidates]), surplus
        for i in candidates:
            addition = min(limit - holding[i], max(1, remaining * weights[i] // pool), surplus)
            holding[i] = holding[i] + addition
            surplus = surplus - addition
    return np.array([limit] + holding)


def uneven(own_key, count, total, reach, slope):
    if count == 2:
        one = jax.random.randint(own_key, (), max(1, total - reach), min(reach, total - 1) + 1)
        return jnp.stack([one, total - one])
    lengths = jnp.asarray(split_up(count, total, reach, slope), jnp.int32)
    couples = (count - 1) // 2
    donor, receiver = lengths[1:1 + 2 * couples:2], lengths[2:2 + 2 * couples:2]
    slack = jnp.minimum(donor - 1, reach - receiver)
    passed = jax.random.randint(jax.random.fold_in(own_key, 1), (couples,), 0, 1 << 20) % (slack + 1)
    lengths = lengths.at[1:1 + 2 * couples:2].set(donor - passed).at[2:2 + 2 * couples:2].set(receiver + passed)
    return lengths[jax.random.permutation(jax.random.fold_in(own_key, 2), count)]


def noise(key, shape, spread, bound, pieces=(), kind=jnp.bfloat16):
    array = jax.random.normal(key, shape, jnp.float32) * spread
    if len(pieces) > 0:
        array = steps_of(key, shape, pieces, -0.22, 0.18) * array
    return jnp.clip(array, min=-bound, max=bound).astype(kind)


def setup_inputs(seed: int = 0) -> dict:
    splits = jax.random.split(jax.random.key(seed), 6)
    theta = noise(splits[0], (S, M, M), 1.0, 6.0, ((1, 64),))
    env_left = noise(splits[1], (W, S * M, M), M ** -0.5, 0.1875, ((0, 8), (1, 64)))
    env_right = noise(splits[2], (W, S * M, M), (M * W) ** -0.5, 0.0390625, ((0, 8), (1, 64)))
    mpo_core = noise(splits[3], (W, W), W ** -0.5, 1.25, (), jnp.float32)
    sector_sizes = uneven(splits[4], S, S * M * 3 // 4, M, 2).astype(jnp.int32)
    return dict(theta=theta, env_left=env_left, env_right=env_right, mpo_core=mpo_core, sector_sizes=sector_sizes)


def reference(theta, env_left, env_right, mpo_core, sector_sizes):
    positions = jnp.arange(M, dtype=jnp.int32)

    def per_sector(index):
        live_size = sector_sizes[index]
        keep_row = positions < live_size
        keep_mask = keep_row[:, None] & keep_row[None, :]
        sector_block = jnp.where(keep_mask, theta[index], jnp.zeros((M, M), jnp.bfloat16))
        start_row = (index * M).astype(jnp.int32)
        left_env = lax.dynamic_slice_in_dim(env_left, start_row, M, 1)
        right_env = lax.dynamic_slice_in_dim(env_right, start_row, M, 1)
        product = jnp.einsum('akm,mn->akn', left_env.astype(jnp.float32), sector_block.astype(jnp.float32)).astype(jnp.bfloat16)
        product = lax.optimization_barrier(product)
        mixed = jnp.einsum('ab,akn->bkn', mpo_core, product.astype(jnp.float32), precision=lax.Precision.HIGHEST).astype(jnp.bfloat16)
        mixed = lax.optimization_barrier(mixed)
        sector_out = jnp.einsum('bil,bjl->ij', mixed.astype(jnp.float32), right_env.astype(jnp.float32))
        sector_out = jnp.where(keep_mask, sector_out, jnp.zeros((M, M), jnp.float32))
        return sector_out.astype(jnp.bfloat16)

    blocks = lax.map(per_sector, jnp.arange(S, dtype=jnp.int32))
    return jnp.transpose(blocks, (1, 0, 2)).reshape(M, S * M)
```

```python
import jax
import jax.numpy as jnp
import numpy as np
from jax import lax
from jax.sharding import Mesh, PartitionSpec as P

G = 4


def on_device(theta, env_left, env_right, mpo_core, sector_sizes):
    sectors, rows_local, width = theta.shape
    local_w, slab, _ = env_left.shape
    n_mpo = lax.axis_size("mpo")
    n_sg = lax.axis_size("sg")
    mm = lax.axis_index("mpo")
    sector = lax.axis_index("sg")
    k = lax.axis_index("k")
    live_size = jnp.sum(jnp.where(jnp.arange(sectors, dtype=jnp.int32) == sector, sector_sizes, 0))

    right_all = lax.all_gather(env_right, "k", axis=1, tiled=True)

    per = rows_local // n_mpo
    sel = lax.dynamic_slice_in_dim(theta, mm * per, per, axis=1)
    spread = jnp.broadcast_to(sel[:, None], (sectors, G, per, width)).reshape(sectors * G, per, width)
    part = lax.all_to_all(spread, ("sg", "k"), 0, 0, tiled=True)
    everyone = jnp.broadcast_to(part[None], (n_mpo,) + part.shape)
    gathered = lax.all_to_all(everyone, "mpo", 0, 0, tiled=True)
    block = jnp.transpose(gathered, (1, 0, 2, 3)).reshape(width, width)
    positions = jnp.arange(width, dtype=jnp.int32)
    keep = positions < live_size
    block = jnp.where(keep[:, None] & keep[None, :], block, jnp.zeros_like(block))

    product = jnp.einsum(
        "akm,mn->akn", env_left, block, preferred_element_type=jnp.float32
    ).astype(jnp.bfloat16)
    sub = slab // n_mpo
    product = product.reshape(local_w, n_mpo, sub, width)
    all_a = lax.all_to_all(product, "mpo", 1, 0, tiled=True).reshape(local_w * n_mpo, sub, width)
    mixed = jnp.einsum(
        "ab,akn->bkn", mpo_core, all_a.astype(jnp.float32), precision=lax.Precision.HIGHEST
    ).astype(jnp.bfloat16)
    mixed = mixed.reshape(n_mpo, local_w, sub, width)
    own_b = lax.all_to_all(mixed, "mpo", 0, 0, tiled=False)

    term = jnp.einsum(
        "mbil,bjl->mij", own_b, right_all, preferred_element_type=jnp.float32
    ).reshape(slab, width)
    row_keep = k * slab + jnp.arange(slab, dtype=jnp.int32) < live_size
    term = jnp.where(row_keep[:, None] & keep[None, :], term, jnp.zeros_like(term))
    halves = n_mpo // G
    term = term.reshape(halves, slab // halves, G, slab)
    term = jnp.transpose(term, (2, 0, 1, 3)).reshape(n_mpo, slab // halves, slab)
    result = lax.psum_scatter(term, "mpo", scatter_dimension=0, tiled=True)
    result = result.reshape(slab // halves, slab).astype(jnp.bfloat16)

    pairs = []
    for src_m in range(n_mpo):
        for g in range(n_sg):
            for kk in range(G):
                dst_m = halves * kk + src_m % halves
                dst_k = src_m // halves
                pairs.append(((src_m * n_sg + g) * G + kk, (dst_m * n_sg + g) * G + dst_k))
    return lax.ppermute(result, ("mpo", "sg", "k"), pairs)


def solution(mesh):
    devices = np.asarray(mesh.devices)
    n_mpo, n_sec = devices.shape
    grid = Mesh(devices.reshape(n_mpo, n_sec // G, G), ("mpo", "sg", "k"))
    sec = ("sg", "k")
    return jax.shard_map(
        on_device,
        mesh=grid,
        in_specs=(P(None, sec, None), P("mpo", sec, None), P("mpo", sec, None), P(), P()),
        out_specs=P("mpo", sec),
        check_vma=False,
    )
```

```python
import jax
import jax.numpy as jnp
import numpy as np
from jax import lax
from jax.sharding import Mesh, PartitionSpec as P

G = 4


def on_device(theta, env_left, env_right, mpo_core, sector_sizes):
    sectors, rows_local, width = theta.shape
    local_w, slab, _ = env_left.shape
    n_mpo = lax.axis_size("mpo")
    n_sg = lax.axis_size("sg")
    mm = lax.axis_index("mpo")
    sector = lax.axis_index("sg")
    k = lax.axis_index("k")
    live_size = jnp.sum(jnp.where(jnp.arange(sectors, dtype=jnp.int32) == sector, sector_sizes, 0))

    right_all = lax.all_gather(env_right, "k", axis=1, tiled=True)

    per = width // n_mpo
    sel = lax.dynamic_slice_in_dim(theta, mm * per, per, axis=2)
    spread = jnp.broadcast_to(sel[:, None], (sectors, G, rows_local, per)).reshape(sectors * G, rows_local, per)
    part = lax.all_to_all(spread, ("sg", "k"), 0, 0, tiled=True).reshape(width, per)
    everyone = jnp.broadcast_to(part[None], (n_mpo,) + part.shape)
    block = lax.all_to_all(everyone, "mpo", 0, 2, tiled=True).reshape(width, width)
    positions = jnp.arange(width, dtype=jnp.int32)
    keep = positions < live_size
    block = jnp.where(keep[:, None] & keep[None, :], block, jnp.zeros_like(block))

    product = jnp.einsum(
        "akm,mn->akn", env_left, block, preferred_element_type=jnp.float32
    ).astype(jnp.bfloat16)
    sub = slab // n_mpo
    product = product.reshape(local_w, n_mpo, sub, width)
    all_a = lax.all_to_all(product, "mpo", 1, 0, tiled=True).reshape(local_w * n_mpo, sub, width)
    mixed = jnp.einsum(
        "ab,akn->bkn", mpo_core, all_a.astype(jnp.float32), precision=lax.Precision.HIGHEST
    ).astype(jnp.bfloat16)
    mixed = mixed.reshape(n_mpo, local_w, sub, width)
    own_b = lax.all_to_all(mixed, "mpo", 0, 0, tiled=False)

    term = jnp.einsum(
        "mbil,bjl->mij", own_b, right_all, preferred_element_type=jnp.float32
    ).reshape(slab, width)
    row_keep = k * slab + jnp.arange(slab, dtype=jnp.int32) < live_size
    term = jnp.where(row_keep[:, None] & keep[None, :], term, jnp.zeros_like(term))
    halves = n_mpo // G
    term = term.reshape(halves, slab // halves, G, slab)
    term = jnp.transpose(term, (2, 0, 1, 3)).reshape(n_mpo, slab // halves, slab)
    result = jnp.sum(lax.all_to_all(term, "mpo", 0, 0, tiled=False), axis=0).astype(jnp.bfloat16)

    pairs = []
    for src_m in range(n_mpo):
        for g in range(n_sg):
            for kk in range(G):
                dst_m = halves * kk + src_m % halves
                dst_k = src_m // halves
                pairs.append(((src_m * n_sg + g) * G + kk, (dst_m * n_sg + g) * G + dst_k))
    return lax.ppermute(result, ("mpo", "sg", "k"), pairs)


def solution(mesh):
    devices = np.asarray(mesh.devices)
    n_mpo, n_sec = devices.shape
    grid = Mesh(devices.reshape(n_mpo, n_sec // G, G), ("mpo", "sg", "k"))
    sec = ("sg", "k")
    return jax.shard_map(
        on_device,
        mesh=grid,
        in_specs=(P(None, sec, None), P("mpo", sec, None), P("mpo", sec, None), P(), P()),
        out_specs=P("mpo", sec),
        check_vma=False,
    )
```

```python
import jax
import jax.numpy as jnp
import numpy as np
from jax import lax
from jax.sharding import Mesh, PartitionSpec as P

G = 4


def shifted(array, pairs):
    return lax.ppermute(array, "k", pairs)


def line_gather(block, k):
    ups, downs = [block], [block]
    for step in range(1, G):
        ups.append(shifted(ups[-1], [(i, i + 1) for i in range(step - 1, G - 1)]))
        downs.append(shifted(downs[-1], [(i + 1, i) for i in range(0, G - step)]))

    def placed(kk):
        parts = [ups[kk - p] if p <= kk else downs[p - kk] for p in range(G)]
        return lambda: jnp.concatenate(parts, axis=1)

    return lax.switch(k, [placed(kk) for kk in range(G)])


def on_device(theta, env_left, env_right, mpo_core, sector_sizes):
    sectors, rows_local, width = theta.shape
    local_w, slab, _ = env_left.shape
    n_mpo = lax.axis_size("mpo")
    n_sg = lax.axis_size("sg")
    mm = lax.axis_index("mpo")
    sector = lax.axis_index("sg")
    k = lax.axis_index("k")
    live_size = jnp.sum(jnp.where(jnp.arange(sectors, dtype=jnp.int32) == sector, sector_sizes, 0))

    right_all = line_gather(env_right, k)

    per = width // n_mpo
    sel = lax.dynamic_slice_in_dim(theta, mm * per, per, axis=2)
    spread = jnp.broadcast_to(sel[:, None], (sectors, G, rows_local, per)).reshape(sectors * G, rows_local, per)
    part = lax.all_to_all(spread, ("sg", "k"), 0, 0, tiled=True).reshape(width, per)
    everyone = jnp.broadcast_to(part[None], (n_mpo,) + part.shape)
    block = lax.all_to_all(everyone, "mpo", 0, 2, tiled=True).reshape(width, width)
    positions = jnp.arange(width, dtype=jnp.int32)
    keep = positions < live_size
    block = jnp.where(keep[:, None] & keep[None, :], block, jnp.zeros_like(block))

    product = jnp.einsum(
        "akm,mn->akn", env_left, block, preferred_element_type=jnp.float32
    ).astype(jnp.bfloat16)
    sub = slab // n_mpo
    product = product.reshape(local_w, n_mpo, sub, width)
    all_a = lax.all_to_all(product, "mpo", 1, 0, tiled=True).reshape(local_w * n_mpo, sub, width)
    mixed = jnp.einsum(
        "ab,akn->bkn", mpo_core, all_a.astype(jnp.float32), precision=lax.Precision.HIGHEST
    ).astype(jnp.bfloat16)
    mixed = mixed.reshape(n_mpo, local_w, sub, width)
    own_b = lax.all_to_all(mixed, "mpo", 0, 0, tiled=False)

    term = jnp.einsum(
        "mbil,bjl->mij", own_b, right_all, preferred_element_type=jnp.float32
    ).reshape(slab, width)
    row_keep = k * slab + jnp.arange(slab, dtype=jnp.int32) < live_size
    term = jnp.where(row_keep[:, None] & keep[None, :], term, jnp.zeros_like(term))
    halves = n_mpo // G
    term = term.reshape(halves, slab // halves, G, slab)
    term = jnp.transpose(term, (2, 0, 1, 3)).reshape(n_mpo, slab // halves, slab)
    result = jnp.sum(lax.all_to_all(term, "mpo", 0, 0, tiled=False), axis=0).astype(jnp.bfloat16)

    pairs = []
    for src_m in range(n_mpo):
        for g in range(n_sg):
            for kk in range(G):
                dst_m = halves * kk + src_m % halves
                dst_k = src_m // halves
                pairs.append(((src_m * n_sg + g) * G + kk, (dst_m * n_sg + g) * G + dst_k))
    return lax.ppermute(result, ("mpo", "sg", "k"), pairs)


def solution(mesh):
    devices = np.asarray(mesh.devices)
    n_mpo, n_sec = devices.shape
    grid = Mesh(devices.reshape(n_mpo, n_sec // G, G), ("mpo", "sg", "k"))
    sec = ("sg", "k")
    return jax.shard_map(
        on_device,
        mesh=grid,
        in_specs=(P(None, sec, None), P("mpo", sec, None), P("mpo", sec, None), P(), P()),
        out_specs=P("mpo", sec),
        check_vma=False,
    )
```

```python
import jax
import jax.numpy as jnp
import numpy as np
from jax import lax
from jax.sharding import Mesh, PartitionSpec as P

G = 4


def shifted(array, pairs):
    return lax.ppermute(array, "k", pairs)


def line_blocks(block):
    ups, downs = [block], [block]
    for step in range(1, G):
        ups.append(shifted(ups[-1], [(i, i + 1) for i in range(step - 1, G - 1)]))
        downs.append(shifted(downs[-1], [(i + 1, i) for i in range(0, G - step)]))
    return ups, downs


def body(theta, env_left, env_right, mpo_core, sector_sizes):
    sectors, rows_local, width = theta.shape
    local_w, slab, _ = env_left.shape
    n_mpo = lax.axis_size("mpo")
    n_sg = lax.axis_size("sg")
    mm = lax.axis_index("mpo")
    sector = lax.axis_index("sg")
    k = lax.axis_index("k")
    live_size = jnp.sum(jnp.where(jnp.arange(sectors, dtype=jnp.int32) == sector, sector_sizes, 0))
    sub = slab // n_mpo

    ups, downs = line_blocks(env_right)

    pieces = env_left.reshape(local_w, n_mpo, sub, width)
    got = [lax.dynamic_index_in_dim(pieces, mm, 1, keepdims=False)]
    for t in range(1, n_mpo):
        piece = lax.dynamic_index_in_dim(pieces, (mm + t) % n_mpo, 1, keepdims=False)
        got.append(lax.ppermute(piece, "mpo", [(i, (i + t) % n_mpo) for i in range(n_mpo)]))
    left_rows = jnp.stack(got).reshape(local_w * n_mpo, sub, width)
    a_order = (3 * ((mm - jnp.arange(n_mpo, dtype=jnp.int32)) % n_mpo))[:, None] + jnp.arange(local_w, dtype=jnp.int32)
    core_rows = jnp.take(mpo_core, a_order.reshape(-1), axis=0)

    per = width // n_mpo
    sel = lax.dynamic_slice_in_dim(theta, mm * per, per, axis=2)
    spread = jnp.broadcast_to(sel[:, None], (sectors, G, rows_local, per)).reshape(sectors * G, rows_local, per)
    part = lax.all_to_all(spread, ("sg", "k"), 0, 0, tiled=True).reshape(width, per)
    everyone = jnp.broadcast_to(part[None], (n_mpo,) + part.shape)
    block = lax.all_to_all(everyone, "mpo", 0, 2, tiled=True).reshape(width, width)
    positions = jnp.arange(width, dtype=jnp.int32)
    keep = positions < live_size
    block = jnp.where(keep[:, None] & keep[None, :], block, jnp.zeros_like(block))

    product = jnp.einsum(
        "akm,mn->akn", left_rows, block, preferred_element_type=jnp.float32
    ).astype(jnp.bfloat16)
    mixed = jnp.einsum(
        "ab,akn->bkn", core_rows, product.astype(jnp.float32), precision=lax.Precision.HIGHEST
    ).astype(jnp.bfloat16)
    mixed = mixed.reshape(n_mpo, local_w, sub, width)
    own_b = lax.all_to_all(mixed, "mpo", 0, 0, tiled=False)

    def placed(kk):
        parts = [ups[kk - p] if p <= kk else downs[p - kk] for p in range(G)]
        return lambda: jnp.concatenate(
            [jnp.einsum("mbil,bjl->mij", own_b, f, preferred_element_type=jnp.float32) for f in parts],
            axis=2,
        )

    term = lax.switch(k, [placed(kk) for kk in range(G)]).reshape(slab, width)
    row_keep = k * slab + jnp.arange(slab, dtype=jnp.int32) < live_size
    term = jnp.where(row_keep[:, None] & keep[None, :], term, jnp.zeros_like(term))
    halves = n_mpo // G
    term = term.reshape(halves, slab // halves, G, slab)
    term = jnp.transpose(term, (2, 0, 1, 3)).reshape(n_mpo, slab // halves, slab)
    result = jnp.sum(lax.all_to_all(term, "mpo", 0, 0, tiled=False), axis=0).astype(jnp.bfloat16)

    pairs = []
    for src_m in range(n_mpo):
        for g in range(n_sg):
            for kk in range(G):
                dst_m = halves * kk + src_m % halves
                dst_k = src_m // halves
                pairs.append(((src_m * n_sg + g) * G + kk, (dst_m * n_sg + g) * G + dst_k))
    return lax.ppermute(result, ("mpo", "sg", "k"), pairs)


def solution(mesh):
    devices = np.asarray(mesh.devices)
    n_mpo, n_sec = devices.shape
    grid = Mesh(devices.reshape(n_mpo, n_sec // G, G), ("mpo", "sg", "k"))
    sec = ("sg", "k")
    return jax.shard_map(
        body,
        mesh=grid,
        in_specs=(P(None, sec, None), P("mpo", sec, None), P("mpo", sec, None), P(), P()),
        out_specs=P("mpo", sec),
        check_vma=False,
    )
```

```python
import jax
import jax.numpy as jnp
import numpy as np
from jax import lax
from jax.sharding import Mesh, PartitionSpec as P

G = 4


def shifted(array, pairs):
    return lax.ppermute(array, "k", pairs)


def line_blocks(block):
    ups, downs = [block], [block]
    for step in range(1, G):
        ups.append(shifted(ups[-1], [(i, i + 1) for i in range(step - 1, G - 1)]))
        downs.append(shifted(downs[-1], [(i + 1, i) for i in range(0, G - step)]))
    return ups, downs


def body(theta, env_left, env_right, mpo_core, sector_sizes):
    sectors, rows_local, width = theta.shape
    local_w, slab, _ = env_left.shape
    n_mpo = lax.axis_size("mpo")
    n_sg = lax.axis_size("sg")
    mm = lax.axis_index("mpo")
    sector = lax.axis_index("sg")
    k = lax.axis_index("k")
    live_size = jnp.sum(jnp.where(jnp.arange(sectors, dtype=jnp.int32) == sector, sector_sizes, 0))
    sub = slab // n_mpo

    ups, downs = line_blocks(env_right)

    per = width // n_mpo
    sel = lax.dynamic_slice_in_dim(theta, mm * per, per, axis=2)
    spread = jnp.broadcast_to(sel[:, None], (sectors, G, rows_local, per)).reshape(sectors * G, rows_local, per)
    part = lax.all_to_all(spread, ("sg", "k"), 0, 0, tiled=True).reshape(width, per)
    everyone = jnp.broadcast_to(part[None], (n_mpo,) + part.shape)
    block = lax.all_to_all(everyone, "mpo", 0, 2, tiled=True).reshape(width, width)
    positions = jnp.arange(width, dtype=jnp.int32)
    keep = positions < live_size
    block = jnp.where(keep[:, None] & keep[None, :], block, jnp.zeros_like(block))

    product = jnp.einsum(
        "akm,mn->akn", env_left, block, preferred_element_type=jnp.float32
    ).astype(jnp.bfloat16)
    product = product.reshape(local_w, n_mpo, sub, width)
    all_a = lax.all_to_all(product, "mpo", 1, 0, tiled=True).reshape(local_w * n_mpo, sub, width)
    mixed = jnp.einsum(
        "ab,akn->bkn", mpo_core, all_a.astype(jnp.float32), precision=lax.Precision.HIGHEST
    ).astype(jnp.bfloat16)
    mixed = mixed.reshape(n_mpo, local_w, sub, width)
    own_b = lax.all_to_all(mixed, "mpo", 0, 0, tiled=False)

    def placed(kk):
        parts = [ups[kk - p] if p <= kk else downs[p - kk] for p in range(G)]
        return lambda: jnp.concatenate(
            [jnp.einsum("mbil,bjl->mij", own_b, f, preferred_element_type=jnp.float32) for f in parts],
            axis=2,
        )

    term = lax.switch(k, [placed(kk) for kk in range(G)]).reshape(slab, width)
    row_keep = k * slab + jnp.arange(slab, dtype=jnp.int32) < live_size
    term = jnp.where(row_keep[:, None] & keep[None, :], term, jnp.zeros_like(term))
    halves = n_mpo // G
    term = term.reshape(halves, slab // halves, G, slab)
    term = jnp.transpose(term, (2, 0, 1, 3)).reshape(n_mpo, slab // halves, slab)
    result = jnp.sum(lax.all_to_all(term, "mpo", 0, 0, tiled=False), axis=0).astype(jnp.bfloat16)

    pairs = []
    for src_m in range(n_mpo):
        for g in range(n_sg):
            for kk in range(G):
                dst_m = halves * kk + src_m % halves
                dst_k = src_m // halves
                pairs.append(((src_m * n_sg + g) * G + kk, (dst_m * n_sg + g) * G + dst_k))
    return lax.ppermute(result, ("mpo", "sg", "k"), pairs)


def solution(mesh):
    devices = np.asarray(mesh.devices)
    n_mpo, n_sec = devices.shape
    grid = Mesh(devices.reshape(n_mpo, n_sec // G, G), ("mpo", "sg", "k"))
    sec = ("sg", "k")
    return jax.shard_map(
        body,
        mesh=grid,
        in_specs=(P(None, sec, None), P("mpo", sec, None), P("mpo", sec, None), P(), P()),
        out_specs=P("mpo", sec),
        check_vma=False,
    )
```

```python
import jax
import jax.numpy as jnp
import numpy as np
from jax import lax
from jax.sharding import Mesh, PartitionSpec as P

G = 4


def on_device(theta, env_left, env_right, mpo_core, sector_sizes):
    sectors, rows_local, width = theta.shape
    local_w, slab, _ = env_left.shape
    n_mpo = lax.axis_size("mpo")
    n_sg = lax.axis_size("sg")
    mm = lax.axis_index("mpo")
    sector = lax.axis_index("sg")
    k = lax.axis_index("k")
    live_size = jnp.sum(jnp.where(jnp.arange(sectors, dtype=jnp.int32) == sector, sector_sizes, 0))

    right_all = lax.all_gather(env_right, "k", axis=1, tiled=True)

    per = width // n_mpo
    sel = lax.dynamic_slice_in_dim(theta, mm * per, per, axis=2)
    spread = jnp.broadcast_to(sel[:, None], (sectors, G, rows_local, per)).reshape(sectors * G, rows_local, per)
    part = lax.all_to_all(spread, ("sg", "k"), 0, 0, tiled=True).reshape(width, per)
    everyone = jnp.broadcast_to(part[None], (n_mpo,) + part.shape)
    block = lax.all_to_all(everyone, "mpo", 0, 2, tiled=True).reshape(width, width)
    positions = jnp.arange(width, dtype=jnp.int32)
    keep = positions < live_size
    block = jnp.where(keep[:, None] & keep[None, :], block, jnp.zeros_like(block))

    product = jnp.einsum(
        "akm,mn->akn", env_left, block, preferred_element_type=jnp.float32
    ).astype(jnp.bfloat16)
    sub = slab // n_mpo
    product = product.reshape(local_w, n_mpo, sub, width)
    all_a = lax.all_to_all(product, "mpo", 1, 0, tiled=True).reshape(local_w * n_mpo, sub, width)
    mixed = jnp.einsum(
        "ab,akn->bkn", mpo_core, all_a.astype(jnp.float32), precision=lax.Precision.HIGHEST
    ).astype(jnp.bfloat16)
    mixed = mixed.reshape(n_mpo, local_w, sub, width)
    own_b = lax.all_to_all(mixed, "mpo", 0, 0, tiled=False)

    term = jnp.einsum(
        "mbil,bjl->mij", own_b, right_all, preferred_element_type=jnp.float32
    ).reshape(slab, width)
    row_keep = k * slab + jnp.arange(slab, dtype=jnp.int32) < live_size
    term = jnp.where(row_keep[:, None] & keep[None, :], term, jnp.zeros_like(term))
    halves = n_mpo // G
    term = term.reshape(halves, slab // halves, G, slab)
    term = jnp.transpose(term, (2, 0, 1, 3)).reshape(n_mpo, slab // halves, slab)
    partials = lax.all_to_all(term.astype(jnp.bfloat16), "mpo", 0, 0, tiled=False)
    result = jnp.sum(partials.astype(jnp.float32), axis=0).astype(jnp.bfloat16)

    pairs = []
    for src_m in range(n_mpo):
        for g in range(n_sg):
            for kk in range(G):
                dst_m = halves * kk + src_m % halves
                dst_k = src_m // halves
                pairs.append(((src_m * n_sg + g) * G + kk, (dst_m * n_sg + g) * G + dst_k))
    return lax.ppermute(result, ("mpo", "sg", "k"), pairs)


def solution(mesh):
    devices = np.asarray(mesh.devices)
    n_mpo, n_sec = devices.shape
    grid = Mesh(devices.reshape(n_mpo, n_sec // G, G), ("mpo", "sg", "k"))
    sec = ("sg", "k")
    return jax.shard_map(
        on_device,
        mesh=grid,
        in_specs=(P(None, sec, None), P("mpo", sec, None), P("mpo", sec, None), P(), P()),
        out_specs=P("mpo", sec),
        check_vma=False,
    )
```

```python
import jax
import jax.numpy as jnp
import numpy as np
from jax import lax
from jax.sharding import Mesh, PartitionSpec as P

G = 4
MPO = ("y", "c")


def on_device(theta, env_left, env_right, mpo_core, sector_sizes):
    sectors, rows_local, width = theta.shape
    local_w, slab, _ = env_left.shape
    n_mpo = lax.axis_size(MPO)
    n_sg = lax.axis_size("sg")
    mm = lax.axis_index(MPO)
    sector = lax.axis_index("sg")
    k = lax.axis_index("k")
    live_size = jnp.sum(jnp.where(jnp.arange(sectors, dtype=jnp.int32) == sector, sector_sizes, 0))

    right_all = lax.all_gather(env_right, "k", axis=1, tiled=True)

    per = width // n_mpo
    sel = lax.dynamic_slice_in_dim(theta, mm * per, per, axis=2)
    spread = jnp.broadcast_to(sel[:, None], (sectors, G, rows_local, per)).reshape(sectors * G, rows_local, per)
    part = lax.all_to_all(spread, ("sg", "k"), 0, 0, tiled=True).reshape(width, per)
    everyone = jnp.broadcast_to(part[None], (n_mpo,) + part.shape)
    block = lax.all_to_all(everyone, MPO, 0, 2, tiled=True).reshape(width, width)
    positions = jnp.arange(width, dtype=jnp.int32)
    keep = positions < live_size
    block = jnp.where(keep[:, None] & keep[None, :], block, jnp.zeros_like(block))

    product = jnp.einsum(
        "akm,mn->akn", env_left, block, preferred_element_type=jnp.float32
    ).astype(jnp.bfloat16)
    sub = slab // n_mpo
    product = product.reshape(local_w, n_mpo, sub, width)
    all_a = lax.all_to_all(product, MPO, 1, 0, tiled=True).reshape(local_w * n_mpo, sub, width)
    mixed = jnp.einsum(
        "ab,akn->bkn", mpo_core, all_a.astype(jnp.float32), precision=lax.Precision.HIGHEST
    ).astype(jnp.bfloat16)
    mixed = mixed.reshape(n_mpo, local_w, sub, width)
    own_b = lax.all_to_all(mixed, MPO, 0, 0, tiled=False)

    term = jnp.einsum(
        "mbil,bjl->mij", own_b, right_all, preferred_element_type=jnp.float32
    ).reshape(slab, width)
    row_keep = k * slab + jnp.arange(slab, dtype=jnp.int32) < live_size
    term = jnp.where(row_keep[:, None] & keep[None, :], term, jnp.zeros_like(term))
    halves = n_mpo // G
    term = term.reshape(halves, slab // halves, G, slab)
    term = jnp.transpose(term, (2, 0, 1, 3)).reshape(n_mpo, slab // halves, slab)
    n_c = lax.axis_size("c")
    c = lax.axis_index("c")
    term = term.reshape(n_mpo // n_c, n_c, slab // halves, slab)
    mine = lax.dynamic_index_in_dim(term, c, 1, keepdims=False)
    other = lax.dynamic_index_in_dim(term, 1 - c, 1, keepdims=False)
    pair = mine + lax.ppermute(other, "c", [(0, 1), (1, 0)])
    result = jnp.sum(lax.all_to_all(pair, "y", 0, 0, tiled=False), axis=0).astype(jnp.bfloat16)

    pairs = []
    for src_m in range(n_mpo):
        for g in range(n_sg):
            for kk in range(G):
                dst_m = halves * kk + src_m % halves
                dst_k = src_m // halves
                pairs.append(((src_m * n_sg + g) * G + kk, (dst_m * n_sg + g) * G + dst_k))
    return lax.ppermute(result, MPO + ("sg", "k"), pairs)


def solution(mesh):
    devices = np.asarray(mesh.devices)
    n_mpo, n_sec = devices.shape
    grid = Mesh(devices.reshape(n_mpo // 2, 2, n_sec // G, G), ("y", "c", "sg", "k"))
    sec = ("sg", "k")
    mpo = ("y", "c")
    return jax.shard_map(
        on_device,
        mesh=grid,
        in_specs=(P(None, sec, None), P(mpo, sec, None), P(mpo, sec, None), P(), P()),
        out_specs=P(mpo, sec),
        check_vma=False,
    )
```

```python
import jax
import jax.numpy as jnp
import numpy as np
from jax import lax
from jax.sharding import Mesh, PartitionSpec as P

G = 4


def on_device(theta, env_left, env_right, mpo_core, sector_sizes):
    sectors, rows_local, width = theta.shape
    local_w, slab, _ = env_left.shape
    n_mpo = lax.axis_size("mpo")
    n_sg = lax.axis_size("sg")
    mm = lax.axis_index("mpo")
    sector = lax.axis_index("sg")
    k = lax.axis_index("k")
    live_size = jnp.sum(jnp.where(jnp.arange(sectors, dtype=jnp.int32) == sector, sector_sizes, 0))

    right_all = lax.all_gather(env_right, "k", axis=0, tiled=False)

    per = width // n_mpo
    sel = lax.dynamic_slice_in_dim(theta, mm * per, per, axis=2)
    spread = jnp.broadcast_to(sel[:, None], (sectors, G, rows_local, per)).reshape(sectors * G, rows_local, per)
    part = lax.all_to_all(spread, ("sg", "k"), 0, 0, tiled=True).reshape(width, per)
    everyone = jnp.broadcast_to(part[None], (n_mpo,) + part.shape)
    block = lax.all_to_all(everyone, "mpo", 0, 2, tiled=True).reshape(width, width)
    positions = jnp.arange(width, dtype=jnp.int32)
    keep = positions < live_size
    block = jnp.where(keep[:, None] & keep[None, :], block, jnp.zeros_like(block))

    product = jnp.einsum(
        "akm,mn->akn", env_left, block, preferred_element_type=jnp.float32
    ).astype(jnp.bfloat16)
    sub = slab // n_mpo
    product = product.reshape(local_w, n_mpo, sub, width)
    all_a = lax.all_to_all(product, "mpo", 1, 0, tiled=True).reshape(local_w * n_mpo, sub, width)
    mixed = jnp.einsum(
        "ab,akn->bkn", mpo_core, all_a.astype(jnp.float32), precision=lax.Precision.HIGHEST
    ).astype(jnp.bfloat16)
    mixed = mixed.reshape(n_mpo, local_w, sub, width)
    own_b = lax.all_to_all(mixed, "mpo", 0, 0, tiled=False)

    term = jnp.einsum(
        "mbil,qbjl->miqj", own_b, right_all, preferred_element_type=jnp.float32
    ).reshape(slab, width)
    row_keep = k * slab + jnp.arange(slab, dtype=jnp.int32) < live_size
    term = jnp.where(row_keep[:, None] & keep[None, :], term, jnp.zeros_like(term))
    halves = n_mpo // G
    term = term.reshape(halves, slab // halves, G, slab)
    term = jnp.transpose(term, (2, 0, 1, 3)).reshape(n_mpo, slab // halves, slab)
    result = jnp.sum(lax.all_to_all(term, "mpo", 0, 0, tiled=False), axis=0).astype(jnp.bfloat16)

    pairs = []
    for src_m in range(n_mpo):
        for g in range(n_sg):
            for kk in range(G):
                dst_m = halves * kk + src_m % halves
                dst_k = src_m // halves
                pairs.append(((src_m * n_sg + g) * G + kk, (dst_m * n_sg + g) * G + dst_k))
    return lax.ppermute(result, ("mpo", "sg", "k"), pairs)


def solution(mesh):
    devices = np.asarray(mesh.devices)
    n_mpo, n_sec = devices.shape
    grid = Mesh(devices.reshape(n_mpo, n_sec // G, G), ("mpo", "sg", "k"))
    sec = ("sg", "k")
    return jax.shard_map(
        on_device,
        mesh=grid,
        in_specs=(P(None, sec, None), P("mpo", sec, None), P("mpo", sec, None), P(), P()),
        out_specs=P("mpo", sec),
        check_vma=False,
    )
```

```python
import jax
import jax.numpy as jnp
import numpy as np
from jax import lax
from jax.sharding import Mesh, PartitionSpec as P

G = 4


def on_device(theta, env_left, env_right, mpo_core, sector_sizes):
    sectors, rows_local, width = theta.shape
    local_w, slab, _ = env_left.shape
    n_mpo = lax.axis_size("mpo")
    n_sg = lax.axis_size("sg")
    mm = lax.axis_index("mpo")
    sector = lax.axis_index("sg")
    k = lax.axis_index("k")
    live_size = jnp.sum(jnp.where(jnp.arange(sectors, dtype=jnp.int32) == sector, sector_sizes, 0))

    right_all = lax.all_gather(env_right, "k", axis=0, tiled=False)

    per = width // n_mpo
    sel = lax.dynamic_slice_in_dim(theta, mm * per, per, axis=2)
    spread = jnp.broadcast_to(sel[:, None], (sectors, G, rows_local, per)).reshape(sectors * G, rows_local, per)
    part = lax.all_to_all(spread, ("sg", "k"), 0, 0, tiled=True).reshape(width, per)
    everyone = jnp.broadcast_to(part[None], (n_mpo,) + part.shape)
    block = lax.all_to_all(everyone, "mpo", 0, 2, tiled=True).reshape(width, width)
    positions = jnp.arange(width, dtype=jnp.int32)
    keep = positions < live_size
    block = jnp.where(keep[:, None] & keep[None, :], block, jnp.zeros_like(block))

    product = jnp.einsum(
        "akm,mn->akn", env_left, block, preferred_element_type=jnp.float32
    ).astype(jnp.bfloat16)
    sub = slab // n_mpo
    product = product.reshape(local_w, n_mpo, sub, width)
    all_a = lax.all_to_all(product, "mpo", 1, 0, tiled=True).reshape(local_w * n_mpo, sub, width)
    core_g = mpo_core.reshape(local_w * n_mpo, n_mpo, local_w)
    mixed = jnp.sum(
        core_g[:, :, :, None, None] * all_a.astype(jnp.float32)[:, None, None], axis=0
    ).astype(jnp.bfloat16)
    own_b = lax.all_to_all(mixed, "mpo", 0, 0, tiled=False)

    term = jnp.einsum(
        "mbil,qbjl->miqj", own_b, right_all, preferred_element_type=jnp.float32
    ).reshape(slab, width)
    row_keep = k * slab + jnp.arange(slab, dtype=jnp.int32) < live_size
    term = jnp.where(row_keep[:, None] & keep[None, :], term, jnp.zeros_like(term))
    halves = n_mpo // G
    term = term.reshape(halves, slab // halves, G, slab)
    term = jnp.transpose(term, (2, 0, 1, 3)).reshape(n_mpo, slab // halves, slab)
    result = jnp.sum(lax.all_to_all(term, "mpo", 0, 0, tiled=False), axis=0).astype(jnp.bfloat16)

    pairs = []
    for src_m in range(n_mpo):
        for g in range(n_sg):
            for kk in range(G):
                dst_m = halves * kk + src_m % halves
                dst_k = src_m // halves
                pairs.append(((src_m * n_sg + g) * G + kk, (dst_m * n_sg + g) * G + dst_k))
    return lax.ppermute(result, ("mpo", "sg", "k"), pairs)


def solution(mesh):
    devices = np.asarray(mesh.devices)
    n_mpo, n_sec = devices.shape
    grid = Mesh(devices.reshape(n_mpo, n_sec // G, G), ("mpo", "sg", "k"))
    sec = ("sg", "k")
    return jax.shard_map(
        on_device,
        mesh=grid,
        in_specs=(P(None, sec, None), P("mpo", sec, None), P("mpo", sec, None), P(), P()),
        out_specs=P("mpo", sec),
        check_vma=False,
    )
```

```python
import jax
import jax.numpy as jnp
import numpy as np
from jax import lax
from jax.sharding import Mesh, PartitionSpec as P

G = 4


def on_device(theta, env_left, env_right, mpo_core, sector_sizes):
    sectors, rows_local, width = theta.shape
    local_w, slab, _ = env_left.shape
    n_mpo = lax.axis_size("mpo")
    n_sg = lax.axis_size("sg")
    mm = lax.axis_index("mpo")
    sector = lax.axis_index("sg")
    k = lax.axis_index("k")
    live_size = jnp.sum(jnp.where(jnp.arange(sectors, dtype=jnp.int32) == sector, sector_sizes, 0))

    right_all = lax.all_gather(env_right, "k", axis=0, tiled=False)

    per = width // n_mpo
    sel = lax.dynamic_slice_in_dim(theta, mm * per, per, axis=2)
    spread = jnp.broadcast_to(sel[:, None], (sectors, G, rows_local, per)).reshape(sectors * G, rows_local, per)
    part = lax.all_to_all(spread, ("sg", "k"), 0, 0, tiled=True).reshape(width, per)
    part_t = part.T
    everyone = jnp.broadcast_to(part_t[None], (n_mpo,) + part_t.shape)
    block_t = lax.all_to_all(everyone, "mpo", 0, 0, tiled=True).reshape(width, width)
    positions = jnp.arange(width, dtype=jnp.int32)
    keep = positions < live_size
    block_t = jnp.where(keep[:, None] & keep[None, :], block_t, jnp.zeros_like(block_t))

    product = jnp.einsum(
        "akm,nm->akn", env_left, block_t, preferred_element_type=jnp.float32
    ).astype(jnp.bfloat16)
    sub = slab // n_mpo
    product = product.reshape(local_w, n_mpo, sub, width)
    all_a = lax.all_to_all(product, "mpo", 1, 0, tiled=True).reshape(local_w * n_mpo, sub, width)
    mixed = jnp.einsum(
        "ab,akn->bkn", mpo_core, all_a.astype(jnp.float32), precision=lax.Precision.HIGHEST
    ).astype(jnp.bfloat16)
    mixed = mixed.reshape(n_mpo, local_w, sub, width)
    own_b = lax.all_to_all(mixed, "mpo", 0, 0, tiled=False)

    term = jnp.einsum(
        "mbil,qbjl->miqj", own_b, right_all, preferred_element_type=jnp.float32
    ).reshape(slab, width)
    row_keep = k * slab + jnp.arange(slab, dtype=jnp.int32) < live_size
    term = jnp.where(row_keep[:, None] & keep[None, :], term, jnp.zeros_like(term))
    halves = n_mpo // G
    term = term.reshape(halves, slab // halves, G, slab)
    term = jnp.transpose(term, (2, 0, 1, 3)).reshape(n_mpo, slab // halves, slab)
    result = jnp.sum(lax.all_to_all(term, "mpo", 0, 0, tiled=False), axis=0).astype(jnp.bfloat16)

    pairs = []
    for src_m in range(n_mpo):
        for g in range(n_sg):
            for kk in range(G):
                dst_m = halves * kk + src_m % halves
                dst_k = src_m // halves
                pairs.append(((src_m * n_sg + g) * G + kk, (dst_m * n_sg + g) * G + dst_k))
    return lax.ppermute(result, ("mpo", "sg", "k"), pairs)


def solution(mesh):
    devices = np.asarray(mesh.devices)
    n_mpo, n_sec = devices.shape
    grid = Mesh(devices.reshape(n_mpo, n_sec // G, G), ("mpo", "sg", "k"))
    sec = ("sg", "k")
    return jax.shard_map(
        on_device,
        mesh=grid,
        in_specs=(P(None, sec, None), P("mpo", sec, None), P("mpo", sec, None), P(), P()),
        out_specs=P("mpo", sec),
        check_vma=False,
    )
```

```python
import jax
import jax.numpy as jnp
import numpy as np
from jax import lax
from jax.sharding import Mesh, PartitionSpec as P

G = 4


def on_device(theta, env_left, env_right, mpo_core, sector_sizes):
    sectors, rows_local, width = theta.shape
    local_w, slab, _ = env_left.shape
    n_mpo = lax.axis_size("mpo")
    n_sg = lax.axis_size("sg")
    mm = lax.axis_index("mpo")
    sector = lax.axis_index("sg")
    k = lax.axis_index("k")
    live_size = jnp.sum(jnp.where(jnp.arange(sectors, dtype=jnp.int32) == sector, sector_sizes, 0))

    right_all = lax.all_gather(env_right, "k", axis=0, tiled=False)

    per = width // n_mpo
    sel = lax.dynamic_slice_in_dim(theta, mm * per, per, axis=2)
    spread = jnp.broadcast_to(sel[:, None], (sectors, G, rows_local, per)).reshape(sectors * G, rows_local, per)
    part = lax.all_to_all(spread, ("sg", "k"), 0, 0, tiled=True).reshape(width, per)
    part_t = part.T
    everyone = jnp.broadcast_to(part_t[None], (n_mpo,) + part_t.shape)
    block_t = lax.all_to_all(everyone, "mpo", 0, 0, tiled=True).reshape(width, width)
    positions = jnp.arange(width, dtype=jnp.int32)
    keep = positions < live_size
    block_t = jnp.where(keep[:, None] & keep[None, :], block_t, jnp.zeros_like(block_t))

    product = jnp.einsum(
        "akm,nm->akn", env_left, block_t, preferred_element_type=jnp.float32
    ).astype(jnp.bfloat16)
    sub = slab // n_mpo
    product = product.reshape(local_w, n_mpo, sub, width)
    all_a = lax.all_to_all(product, "mpo", 1, 0, tiled=True).reshape(local_w * n_mpo, sub, width)
    mixed = jnp.einsum(
        "ab,akn->bkn", mpo_core, all_a.astype(jnp.float32), precision=lax.Precision.HIGHEST
    ).astype(jnp.bfloat16)
    mixed = mixed.reshape(n_mpo, local_w, sub, width)
    own_b = lax.all_to_all(mixed, "mpo", 0, 0, tiled=False)

    term = jnp.einsum(
        "mbil,qbjl->miqj", own_b, right_all, preferred_element_type=jnp.float32
    ).reshape(slab, width)
    halves = n_mpo // G
    term = term.reshape(halves, slab // halves, G, slab)
    term = jnp.transpose(term, (2, 0, 1, 3)).reshape(n_mpo, slab // halves, slab)
    summed = jnp.sum(lax.all_to_all(term, "mpo", 0, 0, tiled=False), axis=0)
    rows_out = slab // halves
    out_rows = k * slab + (mm % halves) * rows_out + jnp.arange(rows_out, dtype=jnp.int32)
    out_cols = (mm // halves) * slab + jnp.arange(slab, dtype=jnp.int32)
    out_keep = (out_rows < live_size)[:, None] & (out_cols < live_size)[None, :]
    result = jnp.where(out_keep, summed, jnp.zeros_like(summed)).astype(jnp.bfloat16)

    pairs = []
    for src_m in range(n_mpo):
        for g in range(n_sg):
            for kk in range(G):
                dst_m = halves * kk + src_m % halves
                dst_k = src_m // halves
                pairs.append(((src_m * n_sg + g) * G + kk, (dst_m * n_sg + g) * G + dst_k))
    return lax.ppermute(result, ("mpo", "sg", "k"), pairs)


def solution(mesh):
    devices = np.asarray(mesh.devices)
    n_mpo, n_sec = devices.shape
    grid = Mesh(devices.reshape(n_mpo, n_sec // G, G), ("mpo", "sg", "k"))
    sec = ("sg", "k")
    return jax.shard_map(
        on_device,
        mesh=grid,
        in_specs=(P(None, sec, None), P("mpo", sec, None), P("mpo", sec, None), P(), P()),
        out_specs=P("mpo", sec),
        check_vma=False,
    )
```

```python
import jax
import jax.numpy as jnp
import numpy as np
from jax import lax
from jax.sharding import Mesh, PartitionSpec as P

G = 4


def on_device(theta, env_left, env_right, mpo_core, sector_sizes):
    sectors, rows_local, width = theta.shape
    local_w, slab, _ = env_left.shape
    n_mpo = lax.axis_size("mpo")
    n_sg = lax.axis_size("sg")
    mm = lax.axis_index("mpo")
    sector = lax.axis_index("sg")
    k = lax.axis_index("k")
    live_size = jnp.sum(jnp.where(jnp.arange(sectors, dtype=jnp.int32) == sector, sector_sizes, 0))

    right_keep = k * slab + jnp.arange(slab, dtype=jnp.int32) < live_size
    right_all = lax.all_gather(
        jnp.where(right_keep[None, :, None], env_right, jnp.zeros_like(env_right)), "k", axis=0, tiled=False
    )

    per = width // n_mpo
    sel = lax.dynamic_slice_in_dim(theta, mm * per, per, axis=2)
    spread = jnp.broadcast_to(sel[:, None], (sectors, G, rows_local, per)).reshape(sectors * G, rows_local, per)
    part = lax.all_to_all(spread, ("sg", "k"), 0, 0, tiled=True).reshape(width, per)
    part_t = part.T
    everyone = jnp.broadcast_to(part_t[None], (n_mpo,) + part_t.shape)
    block_t = lax.all_to_all(everyone, "mpo", 0, 0, tiled=True).reshape(width, width)
    positions = jnp.arange(width, dtype=jnp.int32)
    keep = positions < live_size
    block_t = jnp.where(keep[:, None] & keep[None, :], block_t, jnp.zeros_like(block_t))

    product = jnp.einsum(
        "akm,nm->akn", env_left, block_t, preferred_element_type=jnp.float32
    ).astype(jnp.bfloat16)
    sub = slab // n_mpo
    product = product.reshape(local_w, n_mpo, sub, width)
    all_a = lax.all_to_all(product, "mpo", 1, 0, tiled=True).reshape(local_w * n_mpo, sub, width)
    mixed = jnp.einsum(
        "ab,akn->bkn", mpo_core, all_a.astype(jnp.float32), precision=lax.Precision.HIGHEST
    ).astype(jnp.bfloat16)
    mixed_keep = k * slab + mm * sub + jnp.arange(sub, dtype=jnp.int32) < live_size
    mixed = jnp.where(mixed_keep[None, :, None], mixed, jnp.zeros_like(mixed))
    mixed = mixed.reshape(n_mpo, local_w, sub, width)
    own_b = lax.all_to_all(mixed, "mpo", 0, 0, tiled=False)

    term = jnp.einsum(
        "mbil,qbjl->miqj", own_b, right_all, preferred_element_type=jnp.float32
    ).reshape(slab, width)
    halves = n_mpo // G
    term = term.reshape(halves, slab // halves, G, slab)
    term = jnp.transpose(term, (2, 0, 1, 3)).reshape(n_mpo, slab // halves, slab)
    result = jnp.sum(lax.all_to_all(term, "mpo", 0, 0, tiled=False), axis=0).astype(jnp.bfloat16)

    pairs = []
    for src_m in range(n_mpo):
        for g in range(n_sg):
            for kk in range(G):
                dst_m = halves * kk + src_m % halves
                dst_k = src_m // halves
                pairs.append(((src_m * n_sg + g) * G + kk, (dst_m * n_sg + g) * G + dst_k))
    return lax.ppermute(result, ("mpo", "sg", "k"), pairs)


def solution(mesh):
    devices = np.asarray(mesh.devices)
    n_mpo, n_sec = devices.shape
    grid = Mesh(devices.reshape(n_mpo, n_sec // G, G), ("mpo", "sg", "k"))
    sec = ("sg", "k")
    return jax.shard_map(
        on_device,
        mesh=grid,
        in_specs=(P(None, sec, None), P("mpo", sec, None), P("mpo", sec, None), P(), P()),
        out_specs=P("mpo", sec),
        check_vma=False,
    )
```
